32 devices in a mesh: node: 8 (over y, x, core), feat: 4 (over z).
Axes of the slice: x: 2, y: 2, z: 4, core: 2. Of those that a mesh axis runs over, the one named last changes fastest.
Arguments:
- features: bfloat16 [8192, 512], P('node', 'feat'), may hold values from -6 to 6
- tiles: bfloat16 [512, 128, 128], P('node'), may hold values from -0.1875 to 0.1875
- block_row: int32 [512], P('node'), may hold values from 0 to 7
- block_col: int32 [512], P('node'), may hold values from 0 to 15, as said below
- block_rel: int32 [512], P('node'), may hold values from 0 to 255
- send_list: int32 [64, 1], P('node'), may hold values from 0 to 7
- coef: float32 [256, 30], replicated, may hold values from -1 to 1
- bases: bfloat16 [30, 512, 512], P(None, 'feat'), may hold values from -0.25 to 0.25
- self_weight: bfloat16 [512, 512], P('feat'), may hold values from -0.25 to 0.25
- cotangent: bfloat16 [8192, 512], P('node', 'feat'), may hold values from -6 to 6
Outputs:
- layer_out: bfloat16 [8192, 512], P('node', 'feat')
- feature_grad: float32 [8192, 512], P('node', 'feat')
- basis_grad: bfloat16 [30, 512, 512], P(None, 'feat')
The draws below stay inside these ranges and needn't reach their ends.
Inputs may be any that keep to these rules, and one draw needn't show every extreme that they name: `block_col`: each partition's 64 blocks name each of its 16 slots at least once. `send_list`: row p * 8 + q names local blocks of partition p.
All inputs are finite; a program needn't handle non-finite values.
Results may differ from the reference program's by a relative error of at most 0.005.
Values may be sent and summed in bfloat16 or wider, within the bound.
No kernel may reach another device: no remote copies, remote signals or barrier semaphores. Data moves between devices by JAX's collectives and lax.ppermute only.
A program may use at most 64 MiB of HBM per device.

```python
import math
import jax
import jax.numpy as jnp
from jax import lax

D = 512
B = 30
R = 256
BLK = 128
SP = 1
NB_DEV = 8
BLOCKS = 64
SLOTS = 16
PAIRS = 64
NODES = 8192
N_NODE = 8


def draw_block_col(key, part):
    key_list = jax.random.split(key, N_NODE)

    def one_list(sub_key):
        key_extra, key_order = jax.random.split(sub_key)
        covered = jnp.arange(SLOTS, dtype=jnp.int32)
        extra_cols = jax.random.randint(key_extra, (BLOCKS - SLOTS,), 0, SLOTS, dtype=jnp.int32)
        return jax.random.permutation(key_order, jnp.concatenate([covered, extra_cols]))
    return jax.vmap(one_list)(key_list).reshape(-1).astype(jnp.int32)


def with_ends(result, stream_key, low, largest):
    longest = result.shape.index(max(result.shape))
    spots = []
    for shift in (0, 1):
        where = [jax.random.randint(jax.random.fold_in(stream_key, axis), (), 0, length) for axis, length in enumerate(result.shape)]
        where[longest] = (where[longest] + shift) % result.shape[longest]
        spots.append(tuple(where))
    return result.at[spots[0]].set(low).at[spots[1]].set(largest)


def steps_of(stream_key, shape, cuts, low, high):
    gain = 1.0
    for dim, parts in cuts:
        heights = jax.random.uniform(jax.random.fold_in(jax.random.fold_in(stream_key, 6), dim), (parts,), jnp.float32, low / len(cuts), high / len(cuts))
        gain = gain * jnp.repeat(jnp.exp(heights), shape[dim] // parts).reshape((-1,) + (1,) * (len(shape) - 1 - dim))
    return gain


def centred(stream_key, extent, deviation, bound, pieces=(), held_as=jnp.bfloat16):
    array = deviation * jax.random.normal(stream_key, extent, jnp.float32)
    if pieces:
        array = array * steps_of(stream_key, extent, pieces, -0.22, 0.18)
    return jnp.clip(array, -bound, bound).astype(held_as)


def setup_inputs(seed: int = 0) -> dict:
    seeds = jax.random.split(jax.random.key(seed), 11)
    return {
        "features": centred(seeds[0], (NODES, D), 1.0, 6.0, ((0, 8), (1, 4))),
        "tiles": centred(seeds[1], (N_NODE * BLOCKS, BLK, BLK), (8 * BLK) ** -0.5, 0.1875, ((0, 8),)),
        "block_row": with_ends(jax.random.randint(seeds[2], (N_NODE * BLOCKS,), 0, NB_DEV), jax.random.fold_in(seeds[2], 1), 0, NB_DEV - 1).astype(jnp.int32),
        "block_col": draw_block_col(jax.random.fold_in(seeds[10], 71), 0),
        "block_rel": with_ends(jax.random.randint(seeds[4], (N_NODE * BLOCKS,), 0, R), jax.random.fold_in(seeds[4], 1), 0, R - 1).astype(jnp.int32),
        "send_list": with_ends(jax.random.randint(seeds[5], (PAIRS, SP), 0, NB_DEV), jax.random.fold_in(seeds[5], 1), 0, NB_DEV - 1).astype(jnp.int32),
        "coef": centred(seeds[6], (R, B), B ** -0.5, 1.0, (), jnp.float32),
        "bases": centred(seeds[7], (B, D, D), D ** -0.5, 0.25, ((1, 4),)),
        "self_weight": centred(seeds[8], (D, D), D ** -0.5, 0.25, ((0, 4),)),
        "cotangent": centred(seeds[9], (NODES, D), 1.0, 6.0, ((0, 8), (1, 4))),
    }


def reference(features, tiles, block_row, block_col, block_rel, send_list, coef, bases, self_weight, cotangent):
    exact_products = lax.Precision.HIGHEST
    all_blocks = features.reshape(N_NODE * NB_DEV, BLK, D)
    owners = features.reshape(N_NODE, NB_DEV, BLK, D)
    all_grads = cotangent.reshape(N_NODE, NB_DEV, BLK, D)
    tile_parts = tiles.reshape(N_NODE, BLOCKS, BLK, BLK)
    row_lists = block_row.reshape(N_NODE, BLOCKS)
    col_lists = block_col.reshape(N_NODE, BLOCKS)
    rel_lists = block_rel.reshape(N_NODE, BLOCKS)
    send_table = send_list.reshape(N_NODE, N_NODE, SP)
    part_ids = jnp.arange(N_NODE, dtype=jnp.int32)
    local_ids = part_ids[:, None] * NB_DEV + jnp.arange(NB_DEV, dtype=jnp.int32)[None, :]
    remote_ids = part_ids[:, None, None] * NB_DEV + send_table
    remote_ids = jnp.transpose(remote_ids, (1, 0, 2)).reshape(N_NODE, N_NODE * SP)
    slot_table = jnp.concatenate([local_ids, remote_ids], axis=1).astype(jnp.int32)
    global_cols = jnp.take_along_axis(slot_table, col_lists, axis=1).astype(jnp.int32)
    basis_wide = bases.astype(jnp.float32)
    self_loop_widened = self_weight.astype(jnp.float32)

    def one_partition(running, index_part):
        basis_sum, grad_sum = running
        cols_now = global_cols[index_part]
        source = all_blocks[cols_now].astype(jnp.float32)
        tiles_now = tile_parts[index_part].astype(jnp.float32)
        message = jnp.einsum('kab,kbd->kad', tiles_now, source, precision=exact_products)
        row_select = jax.nn.one_hot(row_lists[index_part], NB_DEV, dtype=jnp.float32)
        block_coef = coef[rel_lists[index_part]]
        summed = jnp.einsum('ki,kb,kad->biad', row_select, block_coef, message, precision=exact_products).astype(jnp.bfloat16)
        summed = lax.optimization_barrier(summed)
        summed_wide = summed.astype(jnp.float32)
        features_widened = owners[index_part].astype(jnp.float32)
        layer_before_bias = jnp.einsum('biad,bde->iae', summed_wide, basis_wide, precision=exact_products)
        layer_before_bias = layer_before_bias + jnp.einsum('qvo,ok->qvk', features_widened, self_loop_widened, precision=exact_products)
        gradients_widened = all_grads[index_part].astype(jnp.float32)
        basis_sum = basis_sum + jnp.einsum('biad,iae->bde', summed_wide, gradients_widened, precision=exact_products)
        grad_summed = jnp.einsum('iae,bde->biad', gradients_widened, basis_wide, precision=exact_products)
        grad_message = jnp.einsum('ki,kb,biad->kad', row_select, block_coef, grad_summed, precision=exact_products).astype(jnp.bfloat16)
        grad_message = lax.optimization_barrier(grad_message).astype(jnp.float32)
        grad_source = jnp.einsum('kab,kad->kbd', tiles_now, grad_message, precision=exact_products)
        grad_sum = grad_sum.at[cols_now].add(grad_source)
        self_loop_gradient = jnp.einsum('bfc,nc->bfn', gradients_widened, self_loop_widened, precision=exact_products)
        grad_sum = grad_sum.at[local_ids[index_part]].add(self_loop_gradient)
        return ((basis_sum, grad_sum), layer_before_bias.astype(jnp.bfloat16))
    start_state = (jnp.zeros((B, D, D), jnp.float32), jnp.zeros((N_NODE * NB_DEV, BLK, D), jnp.float32))
    final_state, layer_parts = lax.scan(one_partition, start_state, part_ids)
    basis_sum, grad_sum = final_state
    layer_out = layer_parts.reshape(NODES, D)
    feature_grad = grad_sum.reshape(NODES, D)
    basis_grad = (basis_sum * (1.0 / math.sqrt(NODES))).astype(jnp.bfloat16)
    return (layer_out, feature_grad, basis_grad)
```

```python
import math

import jax
import jax.numpy as jnp
from jax import lax
from jax.sharding import PartitionSpec as P


def body(
    features, tiles, block_row, block_col, block_rel, send_list, coef, bases, self_weight, cotangent
):
    exact_products = lax.Precision.HIGHEST
    blk_size = tiles.shape[1]
    owned_blocks = features.shape[0] // blk_size
    col_width = features.shape[1]
    partitions = lax.axis_size("node")
    per_peer = send_list.shape[1]
    full_width = bases.shape[2]
    relations = coef.shape[0]
    node_count = owned_blocks * blk_size
    own_cols = jnp.transpose(features.reshape(owned_blocks, blk_size, col_width), (0, 2, 1))
    outgoing = own_cols[send_list]
    remote_rows = lax.all_to_all(outgoing, "node", split_axis=0, concat_axis=0, tiled=True).reshape(
        partitions * per_peer, col_width, blk_size
    )
    slot_rows = jnp.concatenate([own_cols, remote_rows], axis=0)
    slot_count_total = slot_rows.shape[0]
    source = slot_rows[block_col]
    message = jnp.einsum("kab,kcb->kca", tiles, source, preferred_element_type=jnp.float32)
    row_select = (block_row[:, None] == jnp.arange(owned_blocks, dtype=jnp.int32)[None, :]).astype(
        jnp.float32
    )
    rel_select = (block_rel[:, None] == jnp.arange(relations, dtype=jnp.int32)[None, :]).astype(
        jnp.float32
    )
    block_coef = jnp.dot(rel_select, coef, precision=exact_products)
    summed = jnp.einsum(
        "ki,kb,kca->bica", row_select, block_coef, message, precision=exact_products
    ).astype(jnp.bfloat16)
    scale_factor = 1.0 / math.sqrt(partitions * node_count)
    grad_full = lax.all_gather(cotangent, "feat", axis=1, tiled=True).reshape(
        owned_blocks, blk_size, full_width
    )
    basis_part = jnp.einsum("bica,iae->bce", summed, grad_full, preferred_element_type=jnp.float32)
    basis_total = lax.psum(basis_part * scale_factor, "node")
    basis_grad = basis_total.astype(jnp.bfloat16)
    combined = jnp.einsum("bica,bco->oia", summed, bases, preferred_element_type=jnp.float32)
    feat_parts = lax.axis_size("feat")
    out_cols = full_width // feat_parts
    combined = combined.reshape(feat_parts, out_cols, node_count) + jnp.einsum(
        "nc,co->on", features, self_weight, preferred_element_type=jnp.float32
    ).reshape(feat_parts, out_cols, node_count)
    feat_pos = lax.axis_index("feat")
    layer_cols = jnp.take(combined, feat_pos, axis=0)
    for shift in range(1, feat_parts):
        piece = jnp.take(combined, (feat_pos + shift) % feat_parts, axis=0)
        layer_cols = layer_cols + lax.ppermute(
            piece, "feat", [(g, (g + shift) % feat_parts) for g in range(feat_parts)]
        )
    layer_out = jnp.transpose(layer_cols).astype(jnp.bfloat16)
    grad_summed = jnp.einsum("iae,bce->bica", grad_full, bases, preferred_element_type=jnp.float32)
    grad_message = jnp.einsum(
        "ki,kb,bica->kca", row_select, block_coef, grad_summed, precision=exact_products
    ).astype(jnp.bfloat16)
    grad_source = jnp.einsum(
        "kab,kca->kcb", tiles, grad_message, preferred_element_type=jnp.float32
    )
    col_select = (
        block_col[:, None] == jnp.arange(slot_count_total, dtype=jnp.int32)[None, :]
    ).astype(jnp.float32)
    slot_grad = jnp.einsum("ks,kcb->scb", col_select, grad_source, precision=exact_products)
    leaving = slot_grad[owned_blocks:].reshape(partitions, per_peer, col_width, blk_size)
    returned = (
        lax.all_to_all(
            leaving.astype(jnp.bfloat16), "node", split_axis=0, concat_axis=0, tiled=True
        )
        .astype(leaving.dtype)
        .reshape(partitions * per_peer, col_width, blk_size)
    )
    send_select = (
        send_list.reshape(-1)[:, None] == jnp.arange(owned_blocks, dtype=jnp.int32)[None, :]
    ).astype(jnp.float32)
    arrived = jnp.einsum("ti,tcb->icb", send_select, returned, precision=exact_products)
    own_grad = jnp.transpose(slot_grad[:owned_blocks] + arrived, (0, 2, 1))
    self_loop_gradient = jnp.einsum(
        "iae,ce->iac", grad_full, self_weight, preferred_element_type=jnp.float32
    )
    feature_grad = (own_grad + self_loop_gradient).reshape(node_count, col_width)
    return (layer_out, feature_grad, basis_grad)


def solution(mesh):
    return jax.shard_map(
        body,
        mesh=mesh,
        in_specs=(
            P("node", "feat"),
            P("node", None, None),
            P("node"),
            P("node"),
            P("node"),
            P("node", None),
            P(),
            P(None, "feat", None),
            P("feat", None),
            P("node", "feat"),
        ),
        out_specs=(P("node", "feat"), P("node", "feat"), P(None, "feat", None)),
        check_vma=False,
    )
```

```python
import math

import jax
import jax.numpy as jnp
from jax import lax
from jax.sharding import PartitionSpec as P


def body(
    features, tiles, block_row, block_col, block_rel, send_list, coef, bases, self_weight, cotangent
):
    exact_products = lax.Precision.HIGHEST
    blk_size = tiles.shape[1]
    owned_blocks = features.shape[0] // blk_size
    col_width = features.shape[1]
    partitions = lax.axis_size("node")
    per_peer = send_list.shape[1]
    full_width = bases.shape[2]
    relations = coef.shape[0]
    node_count = owned_blocks * blk_size
    own_cols = jnp.transpose(features.reshape(owned_blocks, blk_size, col_width), (0, 2, 1))
    outgoing = own_cols[send_list]
    remote_rows = lax.all_to_all(outgoing, "node", split_axis=0, concat_axis=0, tiled=True).reshape(
        partitions * per_peer, col_width, blk_size
    )
    slot_rows = jnp.concatenate([own_cols, remote_rows], axis=0)
    slot_count_total = slot_rows.shape[0]
    source = slot_rows[block_col]
    message = jnp.einsum("kab,kcb->kca", tiles, source, preferred_element_type=jnp.float32)
    row_select = (block_row[:, None] == jnp.arange(owned_blocks, dtype=jnp.int32)[None, :]).astype(
        jnp.float32
    )
    rel_select = (block_rel[:, None] == jnp.arange(relations, dtype=jnp.int32)[None, :]).astype(
        jnp.float32
    )
    block_coef = jnp.dot(rel_select, coef, precision=exact_products)
    summed = jnp.einsum(
        "ki,kb,kca->bica", row_select, block_coef, message, precision=exact_products
    ).astype(jnp.bfloat16)
    scale_factor = 1.0 / math.sqrt(partitions * node_count)
    grad_full = lax.all_gather(cotangent, "feat", axis=1, tiled=True).reshape(
        owned_blocks, blk_size, full_width
    )
    basis_part = jnp.einsum("bica,iae->bce", summed, grad_full, preferred_element_type=jnp.float32)
    basis_total = lax.psum(basis_part, "node")
    basis_grad = (basis_total * scale_factor).astype(jnp.bfloat16)
    combined = jnp.einsum("bica,bco->oia", summed, bases, preferred_element_type=jnp.float32)
    feat_parts = lax.axis_size("feat")
    out_cols = full_width // feat_parts
    combined = combined.reshape(feat_parts, out_cols, node_count) + jnp.einsum(
        "nc,co->on", features, self_weight, preferred_element_type=jnp.float32
    ).reshape(feat_parts, out_cols, node_count)
    layer_cols = lax.all_to_all(combined, "feat", split_axis=0, concat_axis=0, tiled=True).sum(0)
    layer_out = jnp.transpose(layer_cols).astype(jnp.bfloat16)
    grad_summed = jnp.einsum("iae,bce->bica", grad_full, bases, preferred_element_type=jnp.float32)
    grad_message = jnp.einsum(
        "ki,kb,bica->kca", row_select, block_coef, grad_summed, precision=exact_products
    ).astype(jnp.bfloat16)
    grad_source = jnp.einsum(
        "kab,kca->kcb", tiles, grad_message, preferred_element_type=jnp.float32
    )
    col_select = (
        block_col[:, None] == jnp.arange(slot_count_total, dtype=jnp.int32)[None, :]
    ).astype(jnp.float32)
    slot_grad = jnp.einsum("ks,kcb->scb", col_select, grad_source, precision=exact_products)
    leaving = slot_grad[owned_blocks:].reshape(partitions, per_peer, col_width, blk_size)
    returned = (
        lax.all_to_all(
            leaving.astype(jnp.bfloat16), "node", split_axis=0, concat_axis=0, tiled=True
        )
        .astype(leaving.dtype)
        .reshape(partitions * per_peer, col_width, blk_size)
    )
    send_select = (
        send_list.reshape(-1)[:, None] == jnp.arange(owned_blocks, dtype=jnp.int32)[None, :]
    ).astype(jnp.float32)
    arrived = jnp.einsum("ti,tcb->icb", send_select, returned, precision=exact_products)
    own_grad = jnp.transpose(slot_grad[:owned_blocks] + arrived, (0, 2, 1))
    self_loop_gradient = jnp.einsum(
        "iae,ce->iac", grad_full, self_weight, preferred_element_type=jnp.float32
    )
    feature_grad = (own_grad + self_loop_gradient).reshape(node_count, col_width)
    return (layer_out, feature_grad, basis_grad)


def solution(mesh):
    return jax.shard_map(
        body,
        mesh=mesh,
        in_specs=(
            P("node", "feat"),
            P("node", None, None),
            P("node"),
            P("node"),
            P("node"),
            P("node", None),
            P(),
            P(None, "feat", None),
            P("feat", None),
            P("node", "feat"),
        ),
        out_specs=(P("node", "feat"), P("node", "feat"), P(None, "feat", None)),
        check_vma=False,
    )
```

```python
import math

import jax
import jax.numpy as jnp
from jax import lax
from jax.sharding import PartitionSpec as P


def body(
    features, tiles, block_row, block_col, block_rel, send_list, coef, bases, self_weight, cotangent
):
    exact_products = lax.Precision.HIGHEST
    blk_size = tiles.shape[1]
    owned_blocks = features.shape[0] // blk_size
    col_width = features.shape[1]
    partitions = lax.axis_size("node")
    per_peer = send_list.shape[1]
    full_width = bases.shape[2]
    relations = coef.shape[0]
    node_count = owned_blocks * blk_size
    own_cols = jnp.transpose(features.reshape(owned_blocks, blk_size, col_width), (0, 2, 1))
    outgoing = own_cols[send_list]
    remote_rows = lax.all_to_all(outgoing, "node", split_axis=0, concat_axis=0, tiled=True).reshape(
        partitions * per_peer, col_width, blk_size
    )
    slot_rows = jnp.concatenate([own_cols, remote_rows], axis=0)
    slot_count_total = slot_rows.shape[0]
    source = slot_rows[block_col]
    message = jnp.einsum("kab,kcb->kca", tiles, source, preferred_element_type=jnp.float32)
    row_select = (block_row[:, None] == jnp.arange(owned_blocks, dtype=jnp.int32)[None, :]).astype(
        jnp.float32
    )
    rel_select = (block_rel[:, None] == jnp.arange(relations, dtype=jnp.int32)[None, :]).astype(
        jnp.float32
    )
    block_coef = jnp.dot(rel_select, coef, precision=exact_products)
    summed = jnp.einsum(
        "ki,kb,kca->bica", row_select, block_coef, message, precision=lax.Precision.HIGH
    ).astype(jnp.bfloat16)
    scale_factor = 1.0 / math.sqrt(partitions * node_count)
    grad_full = lax.all_gather(cotangent, "feat", axis=1, tiled=True).reshape(
        owned_blocks, blk_size, full_width
    )
    basis_part = jnp.einsum("bica,iae->bce", summed, grad_full, preferred_element_type=jnp.float32)
    basis_part, summed, grad_full, bases = lax.optimization_barrier(
        (basis_part, summed, grad_full, bases)
    )
    basis_total = lax.psum(basis_part, "node")
    basis_grad = (basis_total * scale_factor).astype(jnp.bfloat16)
    combined = jnp.einsum("bica,bco->oia", summed, bases, preferred_element_type=jnp.float32)
    feat_parts = lax.axis_size("feat")
    out_cols = full_width // feat_parts
    combined = combined.reshape(feat_parts, out_cols, node_count) + jnp.einsum(
        "nc,co->on", features, self_weight, preferred_element_type=jnp.float32
    ).reshape(feat_parts, out_cols, node_count)
    layer_cols = lax.all_to_all(combined, "feat", split_axis=0, concat_axis=0, tiled=True).sum(0)
    layer_out = jnp.transpose(layer_cols).astype(jnp.bfloat16)
    grad_summed = jnp.einsum("iae,bce->bica", grad_full, bases, preferred_element_type=jnp.float32)
    grad_message = jnp.einsum(
        "ki,kb,bica->kca", row_select, block_coef, grad_summed, precision=exact_products
    ).astype(jnp.bfloat16)
    grad_source = jnp.einsum(
        "kab,kca->kcb", tiles, grad_message, preferred_element_type=jnp.float32
    )
    col_select = (
        block_col[:, None] == jnp.arange(slot_count_total, dtype=jnp.int32)[None, :]
    ).astype(jnp.float32)
    slot_grad = jnp.einsum("ks,kcb->scb", col_select, grad_source, precision=exact_products)
    leaving = slot_grad[owned_blocks:].reshape(partitions, per_peer, col_width, blk_size)
    returned = (
        lax.all_to_all(
            leaving.astype(jnp.bfloat16), "node", split_axis=0, concat_axis=0, tiled=True
        )
        .astype(leaving.dtype)
        .reshape(partitions * per_peer, col_width, blk_size)
    )
    send_select = (
        send_list.reshape(-1)[:, None] == jnp.arange(owned_blocks, dtype=jnp.int32)[None, :]
    ).astype(jnp.float32)
    arrived = jnp.einsum("ti,tcb->icb", send_select, returned, precision=exact_products)
    own_grad = jnp.transpose(slot_grad[:owned_blocks] + arrived, (0, 2, 1))
    self_loop_gradient = jnp.einsum(
        "iae,ce->iac", grad_full, self_weight, preferred_element_type=jnp.float32
    )
    feature_grad = (own_grad + self_loop_gradient).reshape(node_count, col_width)
    return (layer_out, feature_grad, basis_grad)


def solution(mesh):
    return jax.shard_map(
        body,
        mesh=mesh,
        in_specs=(
            P("node", "feat"),
            P("node", None, None),
            P("node"),
            P("node"),
            P("node"),
            P("node", None),
            P(),
            P(None, "feat", None),
            P("feat", None),
            P("node", "feat"),
        ),
        out_specs=(P("node", "feat"), P("node", "feat"), P(None, "feat", None)),
        check_vma=False,
    )
```

```python
import math

import jax
import jax.numpy as jnp
from jax import lax
from jax.sharding import PartitionSpec as P


def body(
    features, tiles, block_row, block_col, block_rel, send_list, coef, bases, self_weight, cotangent
):
    exact_products = lax.Precision.HIGHEST
    blk_size = tiles.shape[1]
    owned_blocks = features.shape[0] // blk_size
    col_width = features.shape[1]
    partitions = lax.axis_size("node")
    per_peer = send_list.shape[1]
    full_width = bases.shape[2]
    relations = coef.shape[0]
    node_count = owned_blocks * blk_size
    own_cols = jnp.transpose(features.reshape(owned_blocks, blk_size, col_width), (0, 2, 1))
    outgoing = own_cols[send_list]
    remote_rows = lax.all_to_all(outgoing, "node", split_axis=0, concat_axis=0, tiled=True).reshape(
        partitions * per_peer, col_width, blk_size
    )
    slot_rows = jnp.concatenate([own_cols, remote_rows], axis=0)
    slot_count_total = slot_rows.shape[0]
    source = slot_rows[block_col]
    message = jnp.einsum("kab,kcb->kca", tiles, source, preferred_element_type=jnp.float32)
    row_select = (block_row[:, None] == jnp.arange(owned_blocks, dtype=jnp.int32)[None, :]).astype(
        jnp.float32
    )
    rel_select = (block_rel[:, None] == jnp.arange(relations, dtype=jnp.int32)[None, :]).astype(
        jnp.float32
    )
    block_coef = jnp.dot(rel_select, coef, precision=exact_products)
    block_weight = jnp.einsum("ki,kb->kbi", row_select, block_coef).reshape(row_select.shape[0], -1)
    weight_hi = block_weight.astype(jnp.bfloat16)
    weight_lo = (block_weight - weight_hi.astype(jnp.float32)).astype(jnp.bfloat16)
    weight_three = jnp.concatenate([weight_hi, weight_hi, weight_lo], axis=0)
    message_hi = message.astype(jnp.bfloat16)
    message_lo = (message - message_hi.astype(jnp.float32)).astype(jnp.bfloat16)
    message_three = jnp.concatenate([message_hi, message_lo, message_hi], axis=0)
    summed = (
        jnp.einsum("kx,kca->xca", weight_three, message_three, preferred_element_type=jnp.float32)
        .astype(jnp.bfloat16)
        .reshape(coef.shape[1], owned_blocks, col_width, blk_size)
    )
    scale_factor = 1.0 / math.sqrt(partitions * node_count)
    grad_full = lax.all_gather(cotangent, "feat", axis=1, tiled=True).reshape(
        owned_blocks, blk_size, full_width
    )
    basis_part = jnp.einsum("bica,iae->bce", summed, grad_full, preferred_element_type=jnp.float32)
    basis_part, summed, grad_full, bases = lax.optimization_barrier(
        (basis_part, summed, grad_full, bases)
    )
    basis_total = lax.psum(basis_part, "node")
    basis_grad = (basis_total * scale_factor).astype(jnp.bfloat16)
    combined = jnp.einsum("bica,bco->oia", summed, bases, preferred_element_type=jnp.float32)
    feat_parts = lax.axis_size("feat")
    out_cols = full_width // feat_parts
    combined = combined.reshape(feat_parts, out_cols, node_count) + jnp.einsum(
        "nc,co->on", features, self_weight, preferred_element_type=jnp.float32
    ).reshape(feat_parts, out_cols, node_count)
    layer_cols = lax.all_to_all(combined, "feat", split_axis=0, concat_axis=0, tiled=True).sum(0)
    layer_out = jnp.transpose(layer_cols).astype(jnp.bfloat16)
    grad_summed = jnp.einsum("iae,bce->bica", grad_full, bases, preferred_element_type=jnp.float32)
    grad_message = jnp.einsum(
        "ki,kb,bica->kca", row_select, block_coef, grad_summed, precision=lax.Precision.HIGH
    ).astype(jnp.bfloat16)
    grad_source = jnp.einsum(
        "kab,kca->kcb", tiles, grad_message, preferred_element_type=jnp.float32
    )
    col_select = (
        block_col[:, None] == jnp.arange(slot_count_total, dtype=jnp.int32)[None, :]
    ).astype(jnp.float32)
    slot_grad = jnp.einsum("ks,kcb->scb", col_select, grad_source, precision=exact_products)
    leaving = slot_grad[owned_blocks:].reshape(partitions, per_peer, col_width, blk_size)
    returned = (
        lax.all_to_all(
            leaving.astype(jnp.bfloat16), "node", split_axis=0, concat_axis=0, tiled=True
        )
        .astype(leaving.dtype)
        .reshape(partitions * per_peer, col_width, blk_size)
    )
    send_select = (
        send_list.reshape(-1)[:, None] == jnp.arange(owned_blocks, dtype=jnp.int32)[None, :]
    ).astype(jnp.float32)
    arrived = jnp.einsum("ti,tcb->icb", send_select, returned, precision=exact_products)
    own_grad = jnp.transpose(slot_grad[:owned_blocks] + arrived, (0, 2, 1))
    self_loop_gradient = jnp.einsum(
        "iae,ce->iac", grad_full, self_weight, preferred_element_type=jnp.float32
    )
    feature_grad = (own_grad + self_loop_gradient).reshape(node_count, col_width)
    return (layer_out, feature_grad, basis_grad)


def solution(mesh):
    return jax.shard_map(
        body,
        mesh=mesh,
        in_specs=(
            P("node", "feat"),
            P("node", None, None),
            P("node"),
            P("node"),
            P("node"),
            P("node", None),
            P(),
            P(None, "feat", None),
            P("feat", None),
            P("node", "feat"),
        ),
        out_specs=(P("node", "feat"), P("node", "feat"), P(None, "feat", None)),
        check_vma=False,
    )
```

```python
import math

import jax
import jax.numpy as jnp
from jax import lax
from jax.sharding import PartitionSpec as P


def body(
    features, tiles, block_row, block_col, block_rel, send_list, coef, bases, self_weight, cotangent
):
    exact_products = lax.Precision.HIGHEST
    blk_size = tiles.shape[1]
    owned_blocks = features.shape[0] // blk_size
    col_width = features.shape[1]
    partitions = lax.axis_size("node")
    per_peer = send_list.shape[1]
    full_width = bases.shape[2]
    relations = coef.shape[0]
    node_count = owned_blocks * blk_size
    own_cols = jnp.transpose(features.reshape(owned_blocks, blk_size, col_width), (0, 2, 1))
    outgoing = own_cols[send_list]
    remote_rows = lax.all_to_all(outgoing, "node", split_axis=0, concat_axis=0, tiled=True).reshape(
        partitions * per_peer, col_width, blk_size
    )
    slot_rows = jnp.concatenate([own_cols, remote_rows], axis=0)
    slot_count_total = slot_rows.shape[0]
    source = slot_rows[block_col]
    message = jnp.einsum("kab,kcb->kca", tiles, source, preferred_element_type=jnp.float32)
    row_select = (block_row[:, None] == jnp.arange(owned_blocks, dtype=jnp.int32)[None, :]).astype(
        jnp.float32
    )
    rel_select = (block_rel[:, None] == jnp.arange(relations, dtype=jnp.int32)[None, :]).astype(
        jnp.float32
    )
    block_coef = jnp.dot(rel_select, coef, precision=exact_products)
    summed = jnp.einsum(
        "ki,kb,kca->bica", row_select, block_coef, message, precision=lax.Precision.HIGH
    ).astype(jnp.bfloat16)
    scale_factor = 1.0 / math.sqrt(partitions * node_count)
    grad_full = lax.all_gather(cotangent, "feat", axis=1, tiled=True).reshape(
        owned_blocks, blk_size, full_width
    )
    basis_part = jnp.einsum("bica,iae->bce", summed, grad_full, preferred_element_type=jnp.float32)
    basis_part, summed, grad_full, bases = lax.optimization_barrier(
        (basis_part, summed, grad_full, bases)
    )
    basis_grad = lax.psum((basis_part * scale_factor).astype(jnp.bfloat16), "node")
    combined = jnp.einsum("bica,bco->oia", summed, bases, preferred_element_type=jnp.float32)
    feat_parts = lax.axis_size("feat")
    out_cols = full_width // feat_parts
    combined = combined.reshape(feat_parts, out_cols, node_count) + jnp.einsum(
        "nc,co->on", features, self_weight, preferred_element_type=jnp.float32
    ).reshape(feat_parts, out_cols, node_count)
    layer_cols = lax.all_to_all(combined, "feat", split_axis=0, concat_axis=0, tiled=True).sum(0)
    layer_out = jnp.transpose(layer_cols).astype(jnp.bfloat16)
    grad_summed = jnp.einsum("iae,bce->bica", grad_full, bases, preferred_element_type=jnp.float32)
    grad_message = jnp.einsum(
        "ki,kb,bica->kca", row_select, block_coef, grad_summed, precision=exact_products
    ).astype(jnp.bfloat16)
    grad_source = jnp.einsum(
        "kab,kca->kcb", tiles, grad_message, preferred_element_type=jnp.float32
    )
    col_select = (
        block_col[:, None] == jnp.arange(slot_count_total, dtype=jnp.int32)[None, :]
    ).astype(jnp.float32)
    slot_grad = jnp.einsum("ks,kcb->scb", col_select, grad_source, precision=exact_products)
    leaving = slot_grad[owned_blocks:].reshape(partitions, per_peer, col_width, blk_size)
    returned = (
        lax.all_to_all(
            leaving.astype(jnp.bfloat16), "node", split_axis=0, concat_axis=0, tiled=True
        )
        .astype(leaving.dtype)
        .reshape(partitions * per_peer, col_width, blk_size)
    )
    send_select = (
        send_list.reshape(-1)[:, None] == jnp.arange(owned_blocks, dtype=jnp.int32)[None, :]
    ).astype(jnp.float32)
    arrived = jnp.einsum("ti,tcb->icb", send_select, returned, precision=exact_products)
    own_grad = jnp.transpose(slot_grad[:owned_blocks] + arrived, (0, 2, 1))
    self_loop_gradient = jnp.einsum(
        "iae,ce->iac", grad_full, self_weight, preferred_element_type=jnp.float32
    )
    feature_grad = (own_grad + self_loop_gradient).reshape(node_count, col_width)
    return (layer_out, feature_grad, basis_grad)


def solution(mesh):
    return jax.shard_map(
        body,
        mesh=mesh,
        in_specs=(
            P("node", "feat"),
            P("node", None, None),
            P("node"),
            P("node"),
            P("node"),
            P("node", None),
            P(),
            P(None, "feat", None),
            P("feat", None),
            P("node", "feat"),
        ),
        out_specs=(P("node", "feat"), P("node", "feat"), P(None, "feat", None)),
        check_vma=False,
    )
```

```python
import math

import jax
import jax.numpy as jnp
from jax import lax
from jax.sharding import PartitionSpec as P


def body(
    features, tiles, block_row, block_col, block_rel, send_list, coef, bases, self_weight, cotangent
):
    exact_products = lax.Precision.HIGHEST
    blk_size = tiles.shape[1]
    owned_blocks = features.shape[0] // blk_size
    col_width = features.shape[1]
    partitions = lax.axis_size("node")
    per_peer = send_list.shape[1]
    full_width = bases.shape[2]
    relations = coef.shape[0]
    node_count = owned_blocks * blk_size
    own_cols = jnp.transpose(features.reshape(owned_blocks, blk_size, col_width), (0, 2, 1))
    outgoing = own_cols[send_list]
    remote_rows = lax.all_to_all(outgoing, "node", split_axis=0, concat_axis=0, tiled=True).reshape(
        partitions * per_peer, col_width, blk_size
    )
    slot_rows = jnp.concatenate([own_cols, remote_rows], axis=0)
    slot_count_total = slot_rows.shape[0]
    source = slot_rows[block_col]
    message = jnp.einsum("kab,kcb->kca", tiles, source, preferred_element_type=jnp.float32)
    row_select = (block_row[:, None] == jnp.arange(owned_blocks, dtype=jnp.int32)[None, :]).astype(
        jnp.float32
    )
    rel_select = (block_rel[:, None] == jnp.arange(relations, dtype=jnp.int32)[None, :]).astype(
        jnp.float32
    )
    block_coef = coef[block_rel]
    summed = jnp.einsum(
        "ki,kb,kca->bica", row_select, block_coef, message, precision=lax.Precision.HIGH
    ).astype(jnp.bfloat16)
    scale_factor = 1.0 / math.sqrt(partitions * node_count)
    grad_full = lax.all_gather(cotangent, "feat", axis=1, tiled=True).reshape(
        owned_blocks, blk_size, full_width
    )
    basis_part = jnp.einsum("bica,iae->bce", summed, grad_full, preferred_element_type=jnp.float32)
    basis_part, summed, grad_full, bases = lax.optimization_barrier(
        (basis_part, summed, grad_full, bases)
    )
    basis_total = lax.psum(basis_part, "node")
    basis_grad = (basis_total * scale_factor).astype(jnp.bfloat16)
    combined = jnp.einsum("bica,bco->oia", summed, bases, preferred_element_type=jnp.float32)
    feat_parts = lax.axis_size("feat")
    out_cols = full_width // feat_parts
    combined = combined.reshape(feat_parts, out_cols, node_count) + jnp.einsum(
        "nc,co->on", features, self_weight, preferred_element_type=jnp.float32
    ).reshape(feat_parts, out_cols, node_count)
    layer_cols = lax.all_to_all(combined, "feat", split_axis=0, concat_axis=0, tiled=True).sum(0)
    layer_out = jnp.transpose(layer_cols).astype(jnp.bfloat16)
    grad_summed = jnp.einsum("iae,bce->bica", grad_full, bases, preferred_element_type=jnp.float32)
    grad_message = jnp.einsum(
        "ki,kb,bica->kca", row_select, block_coef, grad_summed, precision=lax.Precision.HIGH
    ).astype(jnp.bfloat16)
    grad_source = jnp.einsum(
        "kab,kca->kcb", tiles, grad_message, preferred_element_type=jnp.float32
    )
    col_select = (
        block_col[:, None] == jnp.arange(slot_count_total, dtype=jnp.int32)[None, :]
    ).astype(jnp.float32)
    slot_grad = jnp.zeros((slot_count_total,) + grad_source.shape[1:], jnp.float32).at[block_col].add(
        grad_source
    )
    leaving = slot_grad[owned_blocks:].reshape(partitions, per_peer, col_width, blk_size)
    returned = (
        lax.all_to_all(
            leaving.astype(jnp.bfloat16), "node", split_axis=0, concat_axis=0, tiled=True
        )
        .astype(leaving.dtype)
        .reshape(partitions * per_peer, col_width, blk_size)
    )
    send_select = (
        send_list.reshape(-1)[:, None] == jnp.arange(owned_blocks, dtype=jnp.int32)[None, :]
    ).astype(jnp.float32)
    arrived = jnp.zeros((owned_blocks,) + returned.shape[1:], jnp.float32).at[send_list.reshape(-1)].add(
        returned
    )
    own_grad = jnp.transpose(slot_grad[:owned_blocks] + arrived, (0, 2, 1))
    self_loop_gradient = jnp.einsum(
        "iae,ce->iac", grad_full, self_weight, preferred_element_type=jnp.float32
    )
    feature_grad = (own_grad + self_loop_gradient).reshape(node_count, col_width)
    return (layer_out, feature_grad, basis_grad)


def solution(mesh):
    return jax.shard_map(
        body,
        mesh=mesh,
        in_specs=(
            P("node", "feat"),
            P("node", None, None),
            P("node"),
            P("node"),
            P("node"),
            P("node", None),
            P(),
            P(None, "feat", None),
            P("feat", None),
            P("node", "feat"),
        ),
        out_specs=(P("node", "feat"), P("node", "feat"), P(None, "feat", None)),
        check_vma=False,
    )
```

```python
import math

import jax
import jax.numpy as jnp
from jax import lax
from jax.sharding import PartitionSpec as P


def body(
    features, tiles, block_row, block_col, block_rel, send_list, coef, bases, self_weight, cotangent
):
    exact_products = lax.Precision.HIGHEST
    blk_size = tiles.shape[1]
    owned_blocks = features.shape[0] // blk_size
    col_width = features.shape[1]
    partitions = lax.axis_size("node")
    per_peer = send_list.shape[1]
    full_width = bases.shape[2]
    relations = coef.shape[0]
    node_count = owned_blocks * blk_size
    own_cols = jnp.transpose(features.reshape(owned_blocks, blk_size, col_width), (0, 2, 1))
    outgoing = own_cols[send_list]
    remote_rows = lax.all_to_all(outgoing, "node", split_axis=0, concat_axis=0, tiled=True).reshape(
        partitions * per_peer, col_width, blk_size
    )
    slot_rows = jnp.concatenate([own_cols, remote_rows], axis=0)
    slot_count_total = slot_rows.shape[0]
    source = slot_rows[block_col]
    message = jnp.einsum("kab,kcb->kca", tiles, source, preferred_element_type=jnp.float32)
    row_select = (block_row[:, None] == jnp.arange(owned_blocks, dtype=jnp.int32)[None, :]).astype(
        jnp.float32
    )
    rel_select = (block_rel[:, None] == jnp.arange(relations, dtype=jnp.int32)[None, :]).astype(
        jnp.float32
    )
    block_coef = coef[block_rel]
    summed = jnp.einsum(
        "ki,kb,kca->bcia", row_select, block_coef, message, precision=lax.Precision.HIGH
    ).astype(jnp.bfloat16)
    scale_factor = 1.0 / math.sqrt(partitions * node_count)
    grad_full = lax.all_gather(cotangent, "feat", axis=1, tiled=True).reshape(
        owned_blocks, blk_size, full_width
    )
    basis_part = jnp.einsum("bcia,iae->bce", summed, grad_full, preferred_element_type=jnp.float32)
    basis_part, summed, grad_full, bases = lax.optimization_barrier(
        (basis_part, summed, grad_full, bases)
    )
    basis_total = lax.psum(basis_part, "node")
    basis_grad = (basis_total * scale_factor).astype(jnp.bfloat16)
    combined = jnp.einsum("bcia,bco->oia", summed, bases, preferred_element_type=jnp.float32)
    feat_parts = lax.axis_size("feat")
    out_cols = full_width // feat_parts
    combined = combined.reshape(feat_parts, out_cols, node_count) + jnp.einsum(
        "nc,co->on", features, self_weight, preferred_element_type=jnp.float32
    ).reshape(feat_parts, out_cols, node_count)
    layer_cols = lax.all_to_all(combined, "feat", split_axis=0, concat_axis=0, tiled=True).sum(0)
    layer_out = jnp.transpose(layer_cols).astype(jnp.bfloat16)
    grad_summed = jnp.einsum("iae,bce->bica", grad_full, bases, preferred_element_type=jnp.float32)
    grad_message = jnp.einsum(
        "ki,kb,bica->kca", row_select, block_coef, grad_summed, precision=lax.Precision.HIGH
    ).astype(jnp.bfloat16)
    grad_source = jnp.einsum(
        "kab,kca->kcb", tiles, grad_message, preferred_element_type=jnp.float32
    )
    col_select = (
        block_col[:, None] == jnp.arange(slot_count_total, dtype=jnp.int32)[None, :]
    ).astype(jnp.float32)
    slot_grad = jnp.zeros((slot_count_total,) + grad_source.shape[1:], jnp.float32).at[block_col].add(
        grad_source
    )
    leaving = slot_grad[owned_blocks:].reshape(partitions, per_peer, col_width, blk_size)
    returned = (
        lax.all_to_all(
            leaving.astype(jnp.bfloat16), "node", split_axis=0, concat_axis=0, tiled=True
        )
        .astype(leaving.dtype)
        .reshape(partitions * per_peer, col_width, blk_size)
    )
    send_select = (
        send_list.reshape(-1)[:, None] == jnp.arange(owned_blocks, dtype=jnp.int32)[None, :]
    ).astype(jnp.float32)
    arrived = jnp.zeros((owned_blocks,) + returned.shape[1:], jnp.float32).at[send_list.reshape(-1)].add(
        returned
    )
    own_grad = jnp.transpose(slot_grad[:owned_blocks] + arrived, (0, 2, 1))
    self_loop_gradient = jnp.einsum(
        "iae,ce->iac", grad_full, self_weight, preferred_element_type=jnp.float32
    )
    feature_grad = (own_grad + self_loop_gradient).reshape(node_count, col_width)
    return (layer_out, feature_grad, basis_grad)


def solution(mesh):
    return jax.shard_map(
        body,
        mesh=mesh,
        in_specs=(
            P("node", "feat"),
            P("node", None, None),
            P("node"),
            P("node"),
            P("node"),
            P("node", None),
            P(),
            P(None, "feat", None),
            P("feat", None),
            P("node", "feat"),
        ),
        out_specs=(P("node", "feat"), P("node", "feat"), P(None, "feat", None)),
        check_vma=False,
    )
```

```python
import functools
import math

import jax
import jax.numpy as jnp
from jax import lax
from jax.sharding import Mesh, NamedSharding
from jax.sharding import PartitionSpec as P


def body(
    features, tiles, block_row, block_col, block_rel, send_list, coef, bases, self_weight, cotangent
):
    exact_products = lax.Precision.HIGHEST
    blk_size = tiles.shape[1]
    owned_blocks = features.shape[0] // blk_size
    col_width = features.shape[1]
    partitions = lax.axis_size("node")
    per_peer = send_list.shape[1]
    full_width = bases.shape[2]
    relations = coef.shape[0]
    node_count = owned_blocks * blk_size
    own_cols = jnp.transpose(features.reshape(owned_blocks, blk_size, col_width), (0, 2, 1))
    outgoing = own_cols[send_list]
    remote_rows = lax.all_to_all(outgoing, "node", split_axis=0, concat_axis=0, tiled=True).reshape(
        partitions * per_peer, col_width, blk_size
    )
    slot_rows = jnp.concatenate([own_cols, remote_rows], axis=0)
    slot_count_total = slot_rows.shape[0]
    source = slot_rows[block_col]
    message = jnp.einsum("kab,kcb->kca", tiles, source, preferred_element_type=jnp.float32)
    row_select = (block_row[:, None] == jnp.arange(owned_blocks, dtype=jnp.int32)[None, :]).astype(
        jnp.float32
    )
    rel_select = (block_rel[:, None] == jnp.arange(relations, dtype=jnp.int32)[None, :]).astype(
        jnp.float32
    )
    block_coef = coef[block_rel]
    summed = jnp.einsum(
        "ki,kb,kca->bcia", row_select, block_coef, message, precision=lax.Precision.HIGH
    ).astype(jnp.bfloat16)
    scale_factor = 1.0 / math.sqrt(partitions * node_count)
    grad_full = lax.all_gather(cotangent, "feat", axis=1, tiled=True).reshape(
        owned_blocks, blk_size, full_width
    )
    basis_part = jnp.einsum("bcia,iae->bce", summed, grad_full, preferred_element_type=jnp.float32)
    basis_part, summed, grad_full, bases = lax.optimization_barrier(
        (basis_part, summed, grad_full, bases)
    )
    combined = jnp.einsum("bcia,bco->oia", summed, bases, preferred_element_type=jnp.float32)
    feat_parts = lax.axis_size("feat")
    out_cols = full_width // feat_parts
    combined = combined.reshape(feat_parts, out_cols, node_count) + jnp.einsum(
        "nc,co->on", features, self_weight, preferred_element_type=jnp.float32
    ).reshape(feat_parts, out_cols, node_count)
    layer_cols = lax.all_to_all(combined, "feat", split_axis=0, concat_axis=0, tiled=True).sum(0)
    layer_out = jnp.transpose(layer_cols).astype(jnp.bfloat16)
    grad_summed = jnp.einsum("iae,bce->bica", grad_full, bases, preferred_element_type=jnp.float32)
    grad_message = jnp.einsum(
        "ki,kb,bica->kca", row_select, block_coef, grad_summed, precision=lax.Precision.HIGH
    ).astype(jnp.bfloat16)
    grad_source = jnp.einsum(
        "kab,kca->kcb", tiles, grad_message, preferred_element_type=jnp.float32
    )
    col_select = (
        block_col[:, None] == jnp.arange(slot_count_total, dtype=jnp.int32)[None, :]
    ).astype(jnp.float32)
    slot_grad = jnp.zeros((slot_count_total,) + grad_source.shape[1:], jnp.float32).at[block_col].add(
        grad_source
    )
    leaving = slot_grad[owned_blocks:].reshape(partitions, per_peer, col_width, blk_size)
    returned = (
        lax.all_to_all(
            leaving.astype(jnp.bfloat16), "node", split_axis=0, concat_axis=0, tiled=True
        )
        .astype(leaving.dtype)
        .reshape(partitions * per_peer, col_width, blk_size)
    )
    send_select = (
        send_list.reshape(-1)[:, None] == jnp.arange(owned_blocks, dtype=jnp.int32)[None, :]
    ).astype(jnp.float32)
    arrived = jnp.zeros((owned_blocks,) + returned.shape[1:], jnp.float32).at[send_list.reshape(-1)].add(
        returned
    )
    own_grad = jnp.transpose(slot_grad[:owned_blocks] + arrived, (0, 2, 1))
    self_loop_gradient = jnp.einsum(
        "iae,ce->iac", grad_full, self_weight, preferred_element_type=jnp.float32
    )
    feature_grad = (own_grad + self_loop_gradient).reshape(node_count, col_width)
    return (layer_out, feature_grad, basis_part)


def reduce_pairs(part, scale_factor):
    pos = lax.axis_index("pair")
    half = part.shape[0] // 2
    low, high = part[:half], part[half:]
    got_high = lax.ppermute(high, "pair", [(0, 1)])
    got_low = lax.ppermute(low, "pair", [(1, 0)])
    mine = jnp.where(pos == 0, low + got_low, high + got_high)
    total = (lax.psum(mine, "group") * scale_factor).astype(jnp.bfloat16)
    other = lax.ppermute(total, "pair", [(0, 1), (1, 0)])
    return jnp.where(
        pos == 0, jnp.concatenate([total, other]), jnp.concatenate([other, total])
    )


def reduce_flat(part, scale_factor):
    return (lax.psum(part, "node") * scale_factor).astype(jnp.bfloat16)


def solution(mesh):
    main = jax.shard_map(
        body,
        mesh=mesh,
        in_specs=(
            P("node", "feat"),
            P("node", None, None),
            P("node"),
            P("node"),
            P("node"),
            P("node", None),
            P(),
            P(None, "feat", None),
            P("feat", None),
            P("node", "feat"),
        ),
        out_specs=(P("node", "feat"), P("node", "feat"), P("node", "feat", None)),
        check_vma=False,
    )
    partitions = mesh.shape["node"]

    def run(*args):
        layer_out, feature_grad, parts = main(*args)
        scale_factor = 1.0 / math.sqrt(args[0].shape[0])
        bases_count = args[7].shape[0]
        if partitions % 2 == 0 and bases_count % 2 == 0:
            pair_mesh = Mesh(
                mesh.devices.reshape((partitions // 2, 2) + mesh.devices.shape[1:]),
                ("group", "pair") + tuple(mesh.axis_names[1:]),
            )
            reduce = jax.shard_map(
                functools.partial(reduce_pairs, scale_factor=scale_factor),
                mesh=pair_mesh,
                in_specs=P(("group", "pair"), "feat", None),
                out_specs=P(None, "feat", None),
                check_vma=False,
            )
        else:
            reduce = jax.shard_map(
                functools.partial(reduce_flat, scale_factor=scale_factor),
                mesh=mesh,
                in_specs=P("node", "feat", None),
                out_specs=P(None, "feat", None),
                check_vma=False,
            )
        basis_grad = lax.with_sharding_constraint(
            reduce(parts), NamedSharding(mesh, P(None, "feat", None))
        )
        return layer_out, feature_grad, basis_grad

    return run
```

```python
import functools
import math

import jax
import jax.numpy as jnp
from jax import lax
from jax.sharding import Mesh, NamedSharding
from jax.sharding import PartitionSpec as P


def body(
    features, tiles, block_row, block_col, block_rel, send_list, coef, bases, self_weight, cotangent
):
    exact_products = lax.Precision.HIGHEST
    blk_size = tiles.shape[1]
    owned_blocks = features.shape[0] // blk_size
    col_width = features.shape[1]
    partitions = lax.axis_size("node")
    per_peer = send_list.shape[1]
    full_width = bases.shape[2]
    relations = coef.shape[0]
    node_count = owned_blocks * blk_size
    own_cols = jnp.transpose(features.reshape(owned_blocks, blk_size, col_width), (0, 2, 1))
    outgoing = own_cols[send_list]
    remote_rows = lax.all_to_all(outgoing, "node", split_axis=0, concat_axis=0, tiled=True).reshape(
        partitions * per_peer, col_width, blk_size
    )
    slot_rows = jnp.concatenate([own_cols, remote_rows], axis=0)
    slot_count_total = slot_rows.shape[0]
    source = slot_rows[block_col]
    message = jnp.einsum("kab,kcb->kca", tiles, source, preferred_element_type=jnp.float32)
    row_select = (block_row[:, None] == jnp.arange(owned_blocks, dtype=jnp.int32)[None, :]).astype(
        jnp.float32
    )
    rel_select = (block_rel[:, None] == jnp.arange(relations, dtype=jnp.int32)[None, :]).astype(
        jnp.float32
    )
    block_coef = coef[block_rel]
    summed = jnp.einsum(
        "ki,kb,kca->bcia", row_select, block_coef, message, precision=lax.Precision.HIGH
    ).astype(jnp.bfloat16)
    scale_factor = 1.0 / math.sqrt(partitions * node_count)
    grad_full = lax.all_gather(cotangent, "feat", axis=1, tiled=True).reshape(
        owned_blocks, blk_size, full_width
    )
    basis_part = jnp.einsum("bcia,iae->bce", summed, grad_full, preferred_element_type=jnp.float32)
    basis_part, summed, grad_full, bases = lax.optimization_barrier(
        (basis_part, summed, grad_full, bases)
    )
    combined = jnp.einsum(
        "bcn,bco->on",
        summed.reshape(summed.shape[0], col_width, node_count),
        bases,
        preferred_element_type=jnp.float32,
    )
    feat_parts = lax.axis_size("feat")
    out_cols = full_width // feat_parts
    combined = combined.reshape(feat_parts, out_cols, node_count) + jnp.einsum(
        "nc,co->on", features, self_weight, preferred_element_type=jnp.float32
    ).reshape(feat_parts, out_cols, node_count)
    layer_cols = lax.all_to_all(combined, "feat", split_axis=0, concat_axis=0, tiled=True).sum(0)
    layer_out = jnp.transpose(layer_cols).astype(jnp.bfloat16)
    grad_summed = jnp.einsum("iae,bce->bica", grad_full, bases, preferred_element_type=jnp.float32)
    grad_message = jnp.einsum(
        "ki,kb,bica->kca", row_select, block_coef, grad_summed, precision=lax.Precision.HIGH
    ).astype(jnp.bfloat16)
    grad_source = jnp.einsum(
        "kab,kca->kcb", tiles, grad_message, preferred_element_type=jnp.float32
    )
    col_select = (
        block_col[:, None] == jnp.arange(slot_count_total, dtype=jnp.int32)[None, :]
    ).astype(jnp.float32)
    slot_grad = jnp.einsum("ks,kcb->scb", col_select, grad_source, precision=exact_products)
    leaving = slot_grad[owned_blocks:].reshape(partitions, per_peer, col_width, blk_size)
    returned = (
        lax.all_to_all(
            leaving.astype(jnp.bfloat16), "node", split_axis=0, concat_axis=0, tiled=True
        )
        .astype(leaving.dtype)
        .reshape(partitions * per_peer, col_width, blk_size)
    )
    send_select = (
        send_list.reshape(-1)[:, None] == jnp.arange(owned_blocks, dtype=jnp.int32)[None, :]
    ).astype(jnp.float32)
    arrived = jnp.einsum("ti,tcb->icb", send_select, returned, precision=exact_products)
    own_grad = jnp.transpose(slot_grad[:owned_blocks] + arrived, (0, 2, 1))
    self_loop_gradient = jnp.einsum(
        "iae,ce->iac", grad_full, self_weight, preferred_element_type=jnp.float32
    )
    feature_grad = (own_grad + self_loop_gradient).reshape(node_count, col_width)
    return (layer_out, feature_grad, basis_part)


def reduce_pairs(part, scale_factor):
    pos = lax.axis_index("pair")
    half = part.shape[0] // 2
    keep = lax.dynamic_slice_in_dim(part, pos * half, half, axis=0)
    send = lax.dynamic_slice_in_dim(part, (1 - pos) * half, half, axis=0)
    mine = keep + lax.ppermute(send, "pair", [(0, 1), (1, 0)])
    total = (lax.psum(mine, "group") * scale_factor).astype(jnp.bfloat16)
    other = lax.ppermute(total, "pair", [(0, 1), (1, 0)])
    both = jnp.stack([total, other])
    order = jnp.arange(2, dtype=jnp.int32) ^ pos
    return jnp.take(both, order, axis=0).reshape(part.shape)


def reduce_flat(part, scale_factor):
    return (lax.psum(part, "node") * scale_factor).astype(jnp.bfloat16)


def solution(mesh):
    main = jax.shard_map(
        body,
        mesh=mesh,
        in_specs=(
            P("node", "feat"),
            P("node", None, None),
            P("node"),
            P("node"),
            P("node"),
            P("node", None),
            P(),
            P(None, "feat", None),
            P("feat", None),
            P("node", "feat"),
        ),
        out_specs=(P("node", "feat"), P("node", "feat"), P("node", "feat", None)),
        check_vma=False,
    )
    partitions = mesh.shape["node"]

    def run(*args):
        layer_out, feature_grad, parts = main(*args)
        scale_factor = 1.0 / math.sqrt(args[0].shape[0])
        bases_count = args[7].shape[0]
        if partitions % 2 == 0 and bases_count % 2 == 0:
            pair_mesh = Mesh(
                mesh.devices.reshape((partitions // 2, 2) + mesh.devices.shape[1:]),
                ("group", "pair") + tuple(mesh.axis_names[1:]),
            )
            reduce = jax.shard_map(
                functools.partial(reduce_pairs, scale_factor=scale_factor),
                mesh=pair_mesh,
                in_specs=P(("group", "pair"), "feat", None),
                out_specs=P(None, "feat", None),
                check_vma=False,
            )
        else:
            reduce = jax.shard_map(
                functools.partial(reduce_flat, scale_factor=scale_factor),
                mesh=mesh,
                in_specs=P("node", "feat", None),
                out_specs=P(None, "feat", None),
                check_vma=False,
            )
        basis_grad = lax.with_sharding_constraint(
            reduce(parts), NamedSharding(mesh, P(None, "feat", None))
        )
        return layer_out, feature_grad, basis_grad

    return run
```

```python
import math

import jax
import jax.numpy as jnp
from jax import lax
from jax.sharding import PartitionSpec as P


def body(
    features, tiles, block_row, block_col, block_rel, send_list, coef, bases, self_weight, cotangent
):
    exact_products = lax.Precision.HIGHEST
    blk_size = tiles.shape[1]
    owned_blocks = features.shape[0] // blk_size
    col_width = features.shape[1]
    partitions = lax.axis_size("node")
    per_peer = send_list.shape[1]
    full_width = bases.shape[2]
    relations = coef.shape[0]
    node_count = owned_blocks * blk_size
    own_cols = jnp.transpose(features.reshape(owned_blocks, blk_size, col_width), (0, 2, 1))
    outgoing = own_cols[send_list]
    remote_rows = lax.all_to_all(outgoing, "node", split_axis=0, concat_axis=0, tiled=True).reshape(
        partitions * per_peer, col_width, blk_size
    )
    slot_rows = jnp.concatenate([own_cols, remote_rows], axis=0)
    slot_count_total = slot_rows.shape[0]
    source = slot_rows[block_col]
    message = jnp.einsum("kab,kcb->kca", tiles, source, preferred_element_type=jnp.float32)
    row_select = (block_row[:, None] == jnp.arange(owned_blocks, dtype=jnp.int32)[None, :]).astype(
        jnp.float32
    )
    rel_select = (block_rel[:, None] == jnp.arange(relations, dtype=jnp.int32)[None, :]).astype(
        jnp.float32
    )
    block_coef = coef[block_rel]
    summed = jnp.einsum(
        "ki,kb,kca->bcia", row_select, block_coef, message, precision=lax.Precision.HIGH
    ).astype(jnp.bfloat16)
    scale_factor = 1.0 / math.sqrt(partitions * node_count)
    grad_full = lax.all_gather(cotangent, "feat", axis=1, tiled=True).reshape(
        owned_blocks, blk_size, full_width
    )
    basis_part = jnp.einsum("bcia,iae->bce", summed, grad_full, preferred_element_type=jnp.float32)
    basis_part, summed, grad_full, bases = lax.optimization_barrier(
        (basis_part, summed, grad_full, bases)
    )
    basis_total = lax.psum(basis_part, "node")
    basis_grad = (basis_total * scale_factor).astype(jnp.bfloat16)
    combined = jnp.einsum("bcia,bco->oia", summed, bases, preferred_element_type=jnp.float32)
    feat_parts = lax.axis_size("feat")
    out_cols = full_width // feat_parts
    combined = combined.reshape(feat_parts, out_cols, node_count) + jnp.einsum(
        "nc,co->on", features, self_weight, preferred_element_type=jnp.float32
    ).reshape(feat_parts, out_cols, node_count)
    layer_cols = lax.all_to_all(combined, "feat", split_axis=0, concat_axis=0, tiled=True).sum(0)
    layer_out = jnp.transpose(layer_cols).astype(jnp.bfloat16)
    grad_summed = jnp.einsum("iae,bce->bica", grad_full, bases, preferred_element_type=jnp.float32)
    grad_message = jnp.einsum(
        "ki,kb,bica->kca", row_select, block_coef, grad_summed, preferred_element_type=jnp.float32
    ).astype(jnp.bfloat16)
    grad_source = jnp.einsum(
        "kab,kca->kcb", tiles, grad_message, preferred_element_type=jnp.float32
    )
    col_select = (
        block_col[:, None] == jnp.arange(slot_count_total, dtype=jnp.int32)[None, :]
    ).astype(jnp.float32)
    slot_grad = jnp.zeros((slot_count_total,) + grad_source.shape[1:], jnp.float32).at[block_col].add(
        grad_source
    )
    leaving = slot_grad[owned_blocks:].reshape(partitions, per_peer, col_width, blk_size)
    returned = (
        lax.all_to_all(
            leaving.astype(jnp.bfloat16), "node", split_axis=0, concat_axis=0, tiled=True
        )
        .astype(leaving.dtype)
        .reshape(partitions * per_peer, col_width, blk_size)
    )
    send_select = (
        send_list.reshape(-1)[:, None] == jnp.arange(owned_blocks, dtype=jnp.int32)[None, :]
    ).astype(jnp.float32)
    arrived = jnp.zeros((owned_blocks,) + returned.shape[1:], jnp.float32).at[send_list.reshape(-1)].add(
        returned
    )
    own_grad = jnp.transpose(slot_grad[:owned_blocks] + arrived, (0, 2, 1))
    self_loop_gradient = jnp.einsum(
        "iae,ce->iac", grad_full, self_weight, preferred_element_type=jnp.float32
    )
    feature_grad = (own_grad + self_loop_gradient).reshape(node_count, col_width)
    return (layer_out, feature_grad, basis_grad)


def solution(mesh):
    return jax.shard_map(
        body,
        mesh=mesh,
        in_specs=(
            P("node", "feat"),
            P("node", None, None),
            P("node"),
            P("node"),
            P("node"),
            P("node", None),
            P(),
            P(None, "feat", None),
            P("feat", None),
            P("node", "feat"),
        ),
        out_specs=(P("node", "feat"), P("node", "feat"), P(None, "feat", None)),
        check_vma=False,
    )
```

```python
import functools
import math

import jax
import jax.numpy as jnp
from jax import lax
from jax.sharding import Mesh, NamedSharding
from jax.sharding import PartitionSpec as P


def body(
    features, tiles, block_row, block_col, block_rel, send_list, coef, bases, self_weight, cotangent
):
    exact_products = lax.Precision.HIGHEST
    blk_size = tiles.shape[1]
    owned_blocks = features.shape[0] // blk_size
    col_width = features.shape[1]
    partitions = lax.axis_size("node")
    per_peer = send_list.shape[1]
    full_width = bases.shape[2]
    relations = coef.shape[0]
    node_count = owned_blocks * blk_size
    own_cols = jnp.transpose(features.reshape(owned_blocks, blk_size, col_width), (0, 2, 1))
    outgoing = own_cols[send_list]
    remote_rows = lax.all_to_all(outgoing, "node", split_axis=0, concat_axis=0, tiled=True).reshape(
        partitions * per_peer, col_width, blk_size
    )
    slot_rows = jnp.concatenate([own_cols, remote_rows], axis=0)
    slot_count_total = slot_rows.shape[0]
    source = slot_rows[block_col]
    message = jnp.einsum("kab,kcb->kca", tiles, source, preferred_element_type=jnp.float32)
    row_select = (block_row[:, None] == jnp.arange(owned_blocks, dtype=jnp.int32)[None, :]).astype(
        jnp.float32
    )
    rel_select = (block_rel[:, None] == jnp.arange(relations, dtype=jnp.int32)[None, :]).astype(
        jnp.float32
    )
    block_coef = coef[block_rel]
    summed = jnp.einsum(
        "ki,kb,kca->bcia", row_select, block_coef, message, precision=lax.Precision.HIGH
    ).astype(jnp.bfloat16)
    scale_factor = 1.0 / math.sqrt(partitions * node_count)
    grad_full = lax.all_gather(cotangent, "feat", axis=1, tiled=True).reshape(
        owned_blocks, blk_size, full_width
    )
    bases_count = summed.shape[0]
    if partitions % 2 == 0 and bases_count % 2 == 0:
        half = bases_count // 2
        pos = lax.axis_index("node") % 2
        sent = jnp.einsum(
            "bcia,iae->bce",
            lax.dynamic_slice_in_dim(summed, (1 - pos) * half, half, axis=0),
            grad_full,
            preferred_element_type=jnp.float32,
        )
        received = lax.ppermute(sent, "node", [(i, i ^ 1) for i in range(partitions)])
        basis_part = (
            jnp.einsum(
                "bcia,iae->bce",
                lax.dynamic_slice_in_dim(summed, pos * half, half, axis=0),
                grad_full,
                preferred_element_type=jnp.float32,
            )
            + received
        )
    else:
        basis_part = jnp.einsum(
            "bcia,iae->bce", summed, grad_full, preferred_element_type=jnp.float32
        )
    basis_part, summed, grad_full, bases = lax.optimization_barrier(
        (basis_part, summed, grad_full, bases)
    )
    combined = jnp.einsum("bcia,bco->oia", summed, bases, preferred_element_type=jnp.float32)
    feat_parts = lax.axis_size("feat")
    out_cols = full_width // feat_parts
    combined = combined.reshape(feat_parts, out_cols, node_count) + jnp.einsum(
        "nc,co->on", features, self_weight, preferred_element_type=jnp.float32
    ).reshape(feat_parts, out_cols, node_count)
    layer_cols = lax.all_to_all(combined, "feat", split_axis=0, concat_axis=0, tiled=True).sum(0)
    layer_out = jnp.transpose(layer_cols).astype(jnp.bfloat16)
    grad_summed = jnp.einsum("iae,bce->bica", grad_full, bases, preferred_element_type=jnp.float32)
    grad_message = jnp.einsum(
        "ki,kb,bica->kca", row_select, block_coef, grad_summed, precision=lax.Precision.HIGH
    ).astype(jnp.bfloat16)
    grad_source = jnp.einsum(
        "kab,kca->kcb", tiles, grad_message, preferred_element_type=jnp.float32
    )
    col_select = (
        block_col[:, None] == jnp.arange(slot_count_total, dtype=jnp.int32)[None, :]
    ).astype(jnp.float32)
    slot_grad = jnp.zeros((slot_count_total,) + grad_source.shape[1:], jnp.float32).at[block_col].add(
        grad_source
    )
    leaving = slot_grad[owned_blocks:].reshape(partitions, per_peer, col_width, blk_size)
    returned = (
        lax.all_to_all(
            leaving.astype(jnp.bfloat16), "node", split_axis=0, concat_axis=0, tiled=True
        )
        .astype(leaving.dtype)
        .reshape(partitions * per_peer, col_width, blk_size)
    )
    send_select = (
        send_list.reshape(-1)[:, None] == jnp.arange(owned_blocks, dtype=jnp.int32)[None, :]
    ).astype(jnp.float32)
    arrived = jnp.zeros((owned_blocks,) + returned.shape[1:], jnp.float32).at[send_list.reshape(-1)].add(
        returned
    )
    own_grad = jnp.transpose(slot_grad[:owned_blocks] + arrived, (0, 2, 1))
    self_loop_gradient = jnp.einsum(
        "iae,ce->iac", grad_full, self_weight, preferred_element_type=jnp.float32
    )
    feature_grad = (own_grad + self_loop_gradient).reshape(node_count, col_width)
    return (layer_out, feature_grad, basis_part)


def reduce_pairs(part, scale_factor):
    pos = lax.axis_index("pair")
    total = (lax.psum(part, "group") * scale_factor).astype(jnp.bfloat16)
    other = lax.ppermute(total, "pair", [(0, 1), (1, 0)])
    return lax.cond(
        pos == 0,
        lambda: jnp.concatenate([total, other]),
        lambda: jnp.concatenate([other, total]),
    )


def reduce_flat(part, scale_factor):
    return (lax.psum(part, "node") * scale_factor).astype(jnp.bfloat16)


def solution(mesh):
    main = jax.shard_map(
        body,
        mesh=mesh,
        in_specs=(
            P("node", "feat"),
            P("node", None, None),
            P("node"),
            P("node"),
            P("node"),
            P("node", None),
            P(),
            P(None, "feat", None),
            P("feat", None),
            P("node", "feat"),
        ),
        out_specs=(P("node", "feat"), P("node", "feat"), P("node", "feat", None)),
        check_vma=False,
    )
    partitions = mesh.shape["node"]

    def run(*args):
        layer_out, feature_grad, parts = main(*args)
        scale_factor = 1.0 / math.sqrt(args[0].shape[0])
        if partitions % 2 == 0 and args[7].shape[0] % 2 == 0:
            pair_mesh = Mesh(
                mesh.devices.reshape((partitions // 2, 2) + mesh.devices.shape[1:]),
                ("group", "pair") + tuple(mesh.axis_names[1:]),
            )
            reduce = jax.shard_map(
                functools.partial(reduce_pairs, scale_factor=scale_factor),
                mesh=pair_mesh,
                in_specs=P(("group", "pair"), "feat", None),
                out_specs=P(None, "feat", None),
                check_vma=False,
            )
        else:
            reduce = jax.shard_map(
                functools.partial(reduce_flat, scale_factor=scale_factor),
                mesh=mesh,
                in_specs=P("node", "feat", None),
                out_specs=P(None, "feat", None),
                check_vma=False,
            )
        basis_grad = lax.with_sharding_constraint(
            reduce(parts), NamedSharding(mesh, P(None, "feat", None))
        )
        return layer_out, feature_grad, basis_grad

    return run
```

```python
import functools
import math

import jax
import jax.numpy as jnp
from jax import lax
from jax.sharding import Mesh, NamedSharding
from jax.sharding import PartitionSpec as P


def body(
    features, tiles, block_row, block_col, block_rel, send_list, coef, bases, self_weight, cotangent
):
    exact_products = lax.Precision.HIGHEST
    blk_size = tiles.shape[1]
    owned_blocks = features.shape[0] // blk_size
    col_width = features.shape[1]
    partitions = lax.axis_size("node")
    per_peer = send_list.shape[1]
    full_width = bases.shape[2]
    relations = coef.shape[0]
    node_count = owned_blocks * blk_size
    own_cols = jnp.transpose(features.reshape(owned_blocks, blk_size, col_width), (0, 2, 1))
    outgoing = own_cols[send_list]
    remote_rows = lax.all_to_all(outgoing, "node", split_axis=0, concat_axis=0, tiled=True).reshape(
        partitions * per_peer, col_width, blk_size
    )
    slot_rows = jnp.concatenate([own_cols, remote_rows], axis=0)
    slot_count_total = slot_rows.shape[0]
    source = slot_rows[block_col]
    message = jnp.einsum("kab,kcb->kca", tiles, source, preferred_element_type=jnp.float32)
    row_select = (block_row[:, None] == jnp.arange(owned_blocks, dtype=jnp.int32)[None, :]).astype(
        jnp.float32
    )
    rel_select = (block_rel[:, None] == jnp.arange(relations, dtype=jnp.int32)[None, :]).astype(
        jnp.float32
    )
    block_coef = coef[block_rel]
    summed = jnp.einsum(
        "ki,kb,kca->bcia", row_select, block_coef, message, precision=lax.Precision.HIGH
    ).astype(jnp.bfloat16)
    scale_factor = 1.0 / math.sqrt(partitions * node_count)
    grad_full = lax.all_gather(cotangent, "feat", axis=1, tiled=True).reshape(
        owned_blocks, blk_size, full_width
    )
    bases_count = summed.shape[0]
    if partitions % 2 == 0 and bases_count % 2 == 0:
        half = bases_count // 2
        pos = lax.axis_index("node") % 2
        sent = jnp.einsum(
            "bcia,iae->bce",
            lax.dynamic_slice_in_dim(summed, (1 - pos) * half, half, axis=0),
            grad_full,
            preferred_element_type=jnp.float32,
        )
        received = lax.ppermute(sent, "node", [(i, i ^ 1) for i in range(partitions)])
        basis_part = (
            jnp.einsum(
                "bcia,iae->bce",
                lax.dynamic_slice_in_dim(summed, pos * half, half, axis=0),
                grad_full,
                preferred_element_type=jnp.float32,
            )
            + received
        )
    else:
        basis_part = jnp.einsum(
            "bcia,iae->bce", summed, grad_full, preferred_element_type=jnp.float32
        )
    basis_part, summed, grad_full, bases = lax.optimization_barrier(
        (basis_part, summed, grad_full, bases)
    )
    combined = jnp.einsum("bcia,bco->oia", summed, bases, preferred_element_type=jnp.float32)
    feat_parts = lax.axis_size("feat")
    out_cols = full_width // feat_parts
    combined = combined.reshape(feat_parts, out_cols, node_count) + jnp.einsum(
        "nc,co->on", features, self_weight, preferred_element_type=jnp.float32
    ).reshape(feat_parts, out_cols, node_count)
    layer_cols = (
        lax.all_to_all(
            combined.astype(jnp.bfloat16), "feat", split_axis=0, concat_axis=0, tiled=True
        )
        .astype(jnp.float32)
        .sum(0)
    )
    layer_out = jnp.transpose(layer_cols).astype(jnp.bfloat16)
    grad_summed = jnp.einsum("iae,bce->bica", grad_full, bases, preferred_element_type=jnp.float32)
    grad_message = jnp.einsum(
        "ki,kb,bica->kca", row_select, block_coef, grad_summed, precision=lax.Precision.HIGH
    ).astype(jnp.bfloat16)
    grad_source = jnp.einsum(
        "kab,kca->kcb", tiles, grad_message, preferred_element_type=jnp.float32
    )
    col_select = (
        block_col[:, None] == jnp.arange(slot_count_total, dtype=jnp.int32)[None, :]
    ).astype(jnp.float32)
    slot_grad = jnp.einsum("ks,kcb->scb", col_select, grad_source, precision=exact_products)
    leaving = slot_grad[owned_blocks:].reshape(partitions, per_peer, col_width, blk_size)
    returned = (
        lax.all_to_all(
            leaving.astype(jnp.bfloat16), "node", split_axis=0, concat_axis=0, tiled=True
        )
        .astype(leaving.dtype)
        .reshape(partitions * per_peer, col_width, blk_size)
    )
    send_select = (
        send_list.reshape(-1)[:, None] == jnp.arange(owned_blocks, dtype=jnp.int32)[None, :]
    ).astype(jnp.float32)
    arrived = jnp.einsum("ti,tcb->icb", send_select, returned, precision=exact_products)
    own_grad = jnp.transpose(slot_grad[:owned_blocks] + arrived, (0, 2, 1))
    self_loop_gradient = jnp.einsum(
        "iae,ce->iac", grad_full, self_weight, preferred_element_type=jnp.float32
    )
    feature_grad = (own_grad + self_loop_gradient).reshape(node_count, col_width)
    return (layer_out, feature_grad, basis_part)


def reduce_pairs(part, scale_factor):
    pos = lax.axis_index("pair")
    total = (lax.psum(part, "group") * scale_factor).astype(jnp.bfloat16)
    other = lax.ppermute(total, "pair", [(0, 1), (1, 0)])
    return lax.cond(
        pos == 0,
        lambda: jnp.concatenate([total, other]),
        lambda: jnp.concatenate([other, total]),
    )


def reduce_flat(part, scale_factor):
    return (lax.psum(part, "node") * scale_factor).astype(jnp.bfloat16)


def solution(mesh):
    main = jax.shard_map(
        body,
        mesh=mesh,
        in_specs=(
            P("node", "feat"),
            P("node", None, None),
            P("node"),
            P("node"),
            P("node"),
            P("node", None),
            P(),
            P(None, "feat", None),
            P("feat", None),
            P("node", "feat"),
        ),
        out_specs=(P("node", "feat"), P("node", "feat"), P("node", "feat", None)),
        check_vma=False,
    )
    partitions = mesh.shape["node"]

    def run(*args):
        layer_out, feature_grad, parts = main(*args)
        scale_factor = 1.0 / math.sqrt(args[0].shape[0])
        if partitions % 2 == 0 and args[7].shape[0] % 2 == 0:
            pair_mesh = Mesh(
                mesh.devices.reshape((partitions // 2, 2) + mesh.devices.shape[1:]),
                ("group", "pair") + tuple(mesh.axis_names[1:]),
            )
            reduce = jax.shard_map(
                functools.partial(reduce_pairs, scale_factor=scale_factor),
                mesh=pair_mesh,
                in_specs=P(("group", "pair"), "feat", None),
                out_specs=P(None, "feat", None),
                check_vma=False,
            )
        else:
            reduce = jax.shard_map(
                functools.partial(reduce_flat, scale_factor=scale_factor),
                mesh=mesh,
                in_specs=P("node", "feat", None),
                out_specs=P(None, "feat", None),
                check_vma=False,
            )
        basis_grad = lax.with_sharding_constraint(
            reduce(parts), NamedSharding(mesh, P(None, "feat", None))
        )
        return layer_out, feature_grad, basis_grad

    return run
```

```python
import math

import jax
import jax.numpy as jnp
from jax import lax
from jax.sharding import PartitionSpec as P


def body(
    features, tiles, block_row, block_col, block_rel, send_list, coef, bases, self_weight, cotangent
):
    exact_products = lax.Precision.HIGHEST
    blk_size = tiles.shape[1]
    owned_blocks = features.shape[0] // blk_size
    col_width = features.shape[1]
    partitions = lax.axis_size("node")
    per_peer = send_list.shape[1]
    full_width = bases.shape[2]
    relations = coef.shape[0]
    node_count = owned_blocks * blk_size
    own_cols = jnp.transpose(features.reshape(owned_blocks, blk_size, col_width), (0, 2, 1))
    outgoing = own_cols[send_list]
    remote_rows = lax.all_to_all(outgoing, "node", split_axis=0, concat_axis=0, tiled=True).reshape(
        partitions * per_peer, col_width, blk_size
    )
    slot_rows = jnp.concatenate([own_cols, remote_rows], axis=0)
    slot_count_total = slot_rows.shape[0]
    source = slot_rows[block_col]
    message = jnp.einsum("kab,kcb->kca", tiles, source, preferred_element_type=jnp.float32)
    row_select = (block_row[:, None] == jnp.arange(owned_blocks, dtype=jnp.int32)[None, :]).astype(
        jnp.float32
    )
    rel_select = (block_rel[:, None] == jnp.arange(relations, dtype=jnp.int32)[None, :]).astype(
        jnp.float32
    )
    block_coef = coef[block_rel]
    summed = jnp.einsum(
        "ki,kb,kca->bcia", row_select, block_coef, message, precision=lax.Precision.HIGH
    ).astype(jnp.bfloat16)
    scale_factor = 1.0 / math.sqrt(partitions * node_count)
    feat_count = lax.axis_size("feat")
    grad_full = lax.all_gather(cotangent, "feat", axis=0).reshape(
        feat_count, owned_blocks, blk_size, full_width // feat_count
    )
    basis_part = jnp.einsum(
        "bcia,fiae->bcfe", summed, grad_full, preferred_element_type=jnp.float32
    ).reshape(summed.shape[0], col_width, full_width)
    basis_part, summed, grad_full, bases = lax.optimization_barrier(
        (basis_part, summed, grad_full, bases)
    )
    basis_total = lax.psum(basis_part, "node")
    basis_grad = (basis_total * scale_factor).astype(jnp.bfloat16)
    combined = jnp.einsum("bcia,bco->oia", summed, bases, preferred_element_type=jnp.float32)
    feat_parts = lax.axis_size("feat")
    out_cols = full_width // feat_parts
    combined = combined.reshape(feat_parts, out_cols, node_count) + jnp.einsum(
        "nc,co->on", features, self_weight, preferred_element_type=jnp.float32
    ).reshape(feat_parts, out_cols, node_count)
    layer_cols = lax.all_to_all(combined, "feat", split_axis=0, concat_axis=0, tiled=True).sum(0)
    layer_out = jnp.transpose(layer_cols).astype(jnp.bfloat16)
    grad_summed = jnp.einsum(
        "fiae,bcfe->bica",
        grad_full,
        bases.reshape(bases.shape[0], col_width, feat_count, full_width // feat_count),
        preferred_element_type=jnp.float32,
    )
    grad_message = jnp.einsum(
        "ki,kb,bica->kca", row_select, block_coef, grad_summed, precision=lax.Precision.HIGH
    ).astype(jnp.bfloat16)
    grad_source = jnp.einsum(
        "kab,kca->kcb", tiles, grad_message, preferred_element_type=jnp.float32
    )
    col_select = (
        block_col[:, None] == jnp.arange(slot_count_total, dtype=jnp.int32)[None, :]
    ).astype(jnp.float32)
    slot_grad = jnp.zeros((slot_count_total,) + grad_source.shape[1:], jnp.float32).at[block_col].add(
        grad_source
    )
    leaving = slot_grad[owned_blocks:].reshape(partitions, per_peer, col_width, blk_size)
    returned = (
        lax.all_to_all(
            leaving.astype(jnp.bfloat16), "node", split_axis=0, concat_axis=0, tiled=True
        )
        .astype(leaving.dtype)
        .reshape(partitions * per_peer, col_width, blk_size)
    )
    send_select = (
        send_list.reshape(-1)[:, None] == jnp.arange(owned_blocks, dtype=jnp.int32)[None, :]
    ).astype(jnp.float32)
    arrived = jnp.zeros((owned_blocks,) + returned.shape[1:], jnp.float32).at[send_list.reshape(-1)].add(
        returned
    )
    own_grad = jnp.transpose(slot_grad[:owned_blocks] + arrived, (0, 2, 1))
    self_loop_gradient = jnp.einsum(
        "fiae,cfe->iac",
        grad_full,
        self_weight.reshape(col_width, feat_count, full_width // feat_count),
        preferred_element_type=jnp.float32,
    )
    feature_grad = (own_grad + self_loop_gradient).reshape(node_count, col_width)
    return (layer_out, feature_grad, basis_grad)


def solution(mesh):
    return jax.shard_map(
        body,
        mesh=mesh,
        in_specs=(
            P("node", "feat"),
            P("node", None, None),
            P("node"),
            P("node"),
            P("node"),
            P("node", None),
            P(),
            P(None, "feat", None),
            P("feat", None),
            P("node", "feat"),
        ),
        out_specs=(P("node", "feat"), P("node", "feat"), P(None, "feat", None)),
        check_vma=False,
    )
```
